512 devices in a mesh: row: 16 (over y, core), col: 32 (over z, x).
Axes of the slice: x: 4, y: 8, z: 8, core: 2. Of those that a mesh axis runs over, the one named last changes fastest.
Arguments:
- tokens: bfloat16 [1024, 8192], P('col', 'row'), may hold values from -6 to 6
- gate_weight: bfloat16 [8192, 16384], P('row', 'col'), may hold values from -0.09375 to 0.09375
- up_weight: bfloat16 [8192, 16384], P('row', 'col'), may hold values from -0.09375 to 0.09375
- down_weight: bfloat16 [16384, 8192], P('col', 'row'), may hold values from -0.0625 to 0.0625
- gate_mask: int32 [64, 128], P('row', 'col'), may hold values from 0 to 1, as said below
- up_mask: int32 [64, 128], P('row', 'col'), may hold values from 0 to 1, as said below
- down_mask: int32 [128, 64], P('col', 'row'), may hold values from 0 to 1, as said below
Outputs:
- mixed: bfloat16 [1024, 8192], P('col', 'row')
The draws below stay inside these ranges and needn't reach their ends.
Inputs may be any that keep to these rules, and one draw needn't show every extreme that they name: `gate_mask`: each entry is 0 or 1; the share of ones differs from one block column of hidden units to another. `up_mask`: each entry is 0 or 1; the share of ones differs from one block column of hidden units to another. `down_mask`: each entry is 0 or 1; the share of ones differs from one block row of hidden units to another.
All inputs are finite; a program needn't handle non-finite values.
Results may differ from the reference program's by a relative error of at most 0.0049.
Values may be sent and summed in bfloat16 or wider, within the bound.
No kernel may reach another device: no remote copies, remote signals or barrier semaphores. Data moves between devices by JAX's collectives and lax.ppermute only.
A program may use at most 64 MiB of HBM per device.

```python
import jax
import jax.numpy as jnp

D = 8192
FF = 16384
BLK = 128
TOKENS = 1024
GROUP_W = 512
N_ROW = 16


def draw_gate_mask(key, part):
    levels = jax.random.randint(jax.random.fold_in(key, 101), (1, FF // BLK), 2, 7)
    picked = jax.random.randint(jax.random.fold_in(key, 102), (D // BLK, FF // BLK), 0, 8)
    return (picked < levels).astype(jnp.int32)


def draw_up_mask(key, part):
    levels = jax.random.randint(jax.random.fold_in(key, 201), (1, FF // BLK), 2, 7)
    picked = jax.random.randint(jax.random.fold_in(key, 202), (D // BLK, FF // BLK), 0, 8)
    return (picked < levels).astype(jnp.int32)


def draw_down_mask(key, part):
    levels = jax.random.randint(jax.random.fold_in(key, 301), (FF // BLK, 1), 2, 7)
    picked = jax.random.randint(jax.random.fold_in(key, 302), (FF // BLK, D // BLK), 0, 8)
    return (picked < levels).astype(jnp.int32)


def level_of(own_key, shape, split, least, high):
    loudness, own = 1.0, jax.random.fold_in(own_key, 6)
    for position, blocks in split:
        steps = jnp.exp(jax.random.uniform(jax.random.fold_in(own, position), (blocks,), jnp.float32, least / len(split), high / len(split)))
        loudness = loudness * jnp.repeat(steps, shape[position] // blocks).reshape([-1 if axis == position else 1 for axis in range(len(shape))])
    return loudness


def centred(rng, dims, width, limit, cuts=(), held_as=jnp.bfloat16):
    array = width * jax.random.normal(rng, dims, jnp.float32)
    if cuts:
        array = array * level_of(rng, dims, cuts, -0.22, 0.18)
    return jnp.clip(array, -limit, limit).astype(held_as)


def setup_inputs(seed: int = 0) -> dict:
    splits = jax.random.split(jax.random.key(seed), 8)
    tokens = centred(splits[0], (TOKENS, D), 1.0, 6.0, ((0, 32), (1, 16)))
    gate_weight = centred(splits[1], (D, FF), (D // 2) ** -0.5, 0.09375, ((0, 16), (1, 32)))
    up_weight = centred(splits[2], (D, FF), (D // 2) ** -0.5, 0.09375, ((0, 16), (1, 32)))
    down_weight = centred(splits[3], (FF, D), (FF // 2) ** -0.5, 0.0625, ((0, 32), (1, 16)))
    gate_mask = draw_gate_mask(jax.random.fold_in(splits[7], 71), 0)
    up_mask = draw_up_mask(jax.random.fold_in(splits[7], 71), 0)
    down_mask = draw_down_mask(jax.random.fold_in(splits[7], 71), 0)
    return {"tokens": tokens, "gate_weight": gate_weight, "up_weight": up_weight, "down_weight": down_weight, "gate_mask": gate_mask, "up_mask": up_mask, "down_mask": down_mask}


def widen(block_mask):
    spread = jnp.repeat(jnp.repeat(block_mask, BLK, axis=0), BLK, axis=1)
    return spread.astype(jnp.bfloat16)


def reference(tokens, gate_weight, up_weight, down_weight, gate_mask, up_mask, down_mask):
    gate_eff = gate_weight * widen(gate_mask)
    up_eff = up_weight * widen(up_mask)
    down_eff = down_weight * widen(down_mask)
    gate = jnp.zeros((TOKENS, FF), jnp.float32)
    up = jnp.zeros((TOKENS, FF), jnp.float32)
    for group in range(N_ROW):
        lower = group * GROUP_W
        columns = tokens[:, lower:lower + GROUP_W]
        gate = gate + jnp.dot(columns, gate_eff[lower:lower + GROUP_W], preferred_element_type=jnp.float32)
        up = up + jnp.dot(columns, up_eff[lower:lower + GROUP_W], preferred_element_type=jnp.float32)
    hidden = (jax.nn.silu(gate) * up).astype(jnp.bfloat16)
    return jnp.dot(hidden, down_eff, preferred_element_type=jnp.float32).astype(jnp.bfloat16)
```

```python
import jax
import jax.numpy as jnp
from jax import lax
from jax.sharding import Mesh
from jax.sharding import PartitionSpec as P

BLK = 128

ROW = ("y", "c")
COL = ("z", "x")


def widen(block_mask):
    rows_blocks, cols_blocks = block_mask.shape
    spread = jnp.broadcast_to(block_mask[:, None, :, None], (rows_blocks, BLK, cols_blocks, BLK))
    return spread.reshape(rows_blocks * BLK, cols_blocks * BLK).astype(jnp.bfloat16)


def swiglu(summed, hidden_cols):
    return (jax.nn.silu(summed[:, :hidden_cols]) * summed[:, hidden_cols:]).astype(jnp.bfloat16)


def gather_rows(x, axes):
    for axis in reversed(axes):
        x = lax.all_gather(x, axis, axis=0, tiled=True)
    return x


def on_device(tokens, gate_weight, up_weight, down_weight, gate_mask, up_mask, down_mask):
    hidden_cols = gate_weight.shape[1]
    both_weights = jnp.concatenate(
        [gate_weight * widen(gate_mask), up_weight * widen(up_mask)], axis=1
    )
    down_eff = down_weight * widen(down_mask)
    all_tokens = gather_rows(tokens, COL)
    n_y, n_c = lax.axis_size("y"), lax.axis_size("c")
    rows, feats = all_tokens.shape
    share = rows // (n_y * n_c)
    by_core = all_tokens.reshape(n_y, n_c, share, feats).transpose(1, 0, 2, 3).reshape(rows, feats)
    partial = jnp.dot(by_core, both_weights, preferred_element_type=jnp.float32)
    partial = lax.psum_scatter(partial, "c", scatter_dimension=0, tiled=True)
    summed = lax.psum_scatter(partial, "y", scatter_dimension=0, tiled=True)
    hidden_share = swiglu(summed, hidden_cols)
    hidden = gather_rows(hidden_share, ROW)
    partial_out = jnp.dot(hidden, down_eff, preferred_element_type=jnp.float32)
    for axis in COL:
        partial_out = lax.psum_scatter(partial_out, axis, scatter_dimension=0, tiled=True)
    return partial_out.astype(jnp.bfloat16)


def solution(mesh):
    n_row, n_col = mesh.devices.shape
    n_c = 2
    n_x = 4
    sub = Mesh(
        mesh.devices.reshape(n_row // n_c, n_c, n_col // n_x, n_x), ROW + COL
    )
    placed = (
        P(COL, ROW),
        P(ROW, COL),
        P(ROW, COL),
        P(COL, ROW),
        P(ROW, COL),
        P(ROW, COL),
        P(COL, ROW),
    )
    return jax.shard_map(
        on_device, mesh=sub, in_specs=placed, out_specs=P(COL, ROW), check_vma=False
    )
```

```python
import jax
import jax.numpy as jnp
from jax import lax
from jax.sharding import Mesh
from jax.sharding import PartitionSpec as P

BLK = 128

ROW = ("y", "c")
COL = ("z", "x")


def widen(block_mask):
    rows_blocks, cols_blocks = block_mask.shape
    spread = jnp.broadcast_to(block_mask[:, None, :, None], (rows_blocks, BLK, cols_blocks, BLK))
    return spread.reshape(rows_blocks * BLK, cols_blocks * BLK).astype(jnp.bfloat16)


def swiglu(summed, hidden_cols):
    return (jax.nn.silu(summed[:, :hidden_cols]) * summed[:, hidden_cols:]).astype(jnp.bfloat16)


def gather_a2a(x, axis):
    n = lax.axis_size(axis)
    copies = jnp.broadcast_to(x[None], (n,) + x.shape).reshape((n * x.shape[0],) + x.shape[1:])
    return lax.all_to_all(copies, axis, 0, 0, tiled=True)


def scatter_sum_a2a(x, axis):
    n = lax.axis_size(axis)
    got = lax.all_to_all(x, axis, 0, 0, tiled=True)
    return got.reshape((n, x.shape[0] // n) + x.shape[1:]).sum(axis=0)


def on_device(tokens, gate_weight, up_weight, down_weight, gate_mask, up_mask, down_mask):
    hidden_cols = gate_weight.shape[1]
    both_weights = jnp.concatenate(
        [gate_weight * widen(gate_mask), up_weight * widen(up_mask)], axis=1
    )
    down_eff = down_weight * widen(down_mask)
    all_tokens = gather_a2a(lax.all_gather(tokens, "x", axis=0, tiled=True), "z")
    n_y, n_c = lax.axis_size("y"), lax.axis_size("c")
    rows, feats = all_tokens.shape
    share = rows // (n_y * n_c)
    by_core = all_tokens.reshape(n_y, n_c, share, feats).transpose(1, 0, 2, 3).reshape(rows, feats)
    partial = jnp.dot(by_core, both_weights, preferred_element_type=jnp.float32)
    summed = scatter_sum_a2a(scatter_sum_a2a(partial, "c"), "y")
    hidden_share = swiglu(summed, hidden_cols)
    half = gather_a2a(hidden_share, "y")
    both = lax.all_gather(half, "c", axis=0, tiled=True)
    hidden = both.reshape(n_c, n_y, share, -1).transpose(1, 0, 2, 3).reshape(rows, -1)
    partial_out = jnp.dot(hidden, down_eff, preferred_element_type=jnp.float32)
    partial_out = scatter_sum_a2a(scatter_sum_a2a(partial_out, "z"), "x")
    return partial_out.astype(jnp.bfloat16)


def solution(mesh):
    n_row, n_col = mesh.devices.shape
    n_c = 2
    n_x = 4
    sub = Mesh(
        mesh.devices.reshape(n_row // n_c, n_c, n_col // n_x, n_x), ROW + COL
    )
    placed = (
        P(COL, ROW),
        P(ROW, COL),
        P(ROW, COL),
        P(COL, ROW),
        P(ROW, COL),
        P(ROW, COL),
        P(COL, ROW),
    )
    return jax.shard_map(
        on_device, mesh=sub, in_specs=placed, out_specs=P(COL, ROW), check_vma=False
    )
```

```python
import math

import jax
import jax.numpy as jnp
from jax import lax
from jax.sharding import Mesh
from jax.sharding import PartitionSpec as P

BLK = 128

ROW = ("y", "c")
COL = ("z", "x")


def widen(block_mask):
    rows_blocks, cols_blocks = block_mask.shape
    spread = jnp.broadcast_to(block_mask[:, None, :, None], (rows_blocks, BLK, cols_blocks, BLK))
    return spread.reshape(rows_blocks * BLK, cols_blocks * BLK).astype(jnp.bfloat16)


def swiglu(summed, hidden_cols):
    return (jax.nn.silu(summed[:, :hidden_cols]) * summed[:, hidden_cols:]).astype(jnp.bfloat16)


def group_size(axis):
    axes = axis if isinstance(axis, tuple) else (axis,)
    return math.prod(lax.axis_size(a) for a in axes)


def gather_a2a(x, axis):
    n = group_size(axis)
    copies = jnp.broadcast_to(x[None], (n,) + x.shape).reshape((n * x.shape[0],) + x.shape[1:])
    return lax.all_to_all(copies, axis, 0, 0, tiled=True)


def scatter_sum_a2a(x, axis):
    n = group_size(axis)
    got = lax.all_to_all(x, axis, 0, 0, tiled=True)
    return got.reshape((n, x.shape[0] // n) + x.shape[1:]).sum(axis=0)


def on_device(tokens, gate_weight, up_weight, down_weight, gate_mask, up_mask, down_mask):
    hidden_cols = gate_weight.shape[1]
    both_weights = jnp.concatenate(
        [gate_weight * widen(gate_mask), up_weight * widen(up_mask)], axis=1
    )
    down_eff = down_weight * widen(down_mask)
    all_tokens = gather_a2a(tokens, COL)
    n_y, n_c = lax.axis_size("y"), lax.axis_size("c")
    rows, feats = all_tokens.shape
    share = rows // (n_y * n_c)
    by_core = all_tokens.reshape(n_y, n_c, share, feats).transpose(1, 0, 2, 3).reshape(rows, feats)
    partial = jnp.dot(by_core, both_weights, preferred_element_type=jnp.float32)
    summed = lax.psum_scatter(scatter_sum_a2a(partial, "c"), "y", scatter_dimension=0, tiled=True)
    hidden_share = swiglu(summed, hidden_cols)
    half = gather_a2a(hidden_share, "y")
    both = gather_a2a(half, "c")
    hidden = both.reshape(n_c, n_y, share, -1).transpose(1, 0, 2, 3).reshape(rows, -1)
    partial_out = jnp.dot(hidden, down_eff, preferred_element_type=jnp.float32)
    partial_out = scatter_sum_a2a(lax.psum_scatter(partial_out, "z", scatter_dimension=0, tiled=True), "x")
    return partial_out.astype(jnp.bfloat16)


def solution(mesh):
    n_row, n_col = mesh.devices.shape
    n_c = 2
    n_x = 4
    sub = Mesh(
        mesh.devices.reshape(n_row // n_c, n_c, n_col // n_x, n_x), ROW + COL
    )
    placed = (
        P(COL, ROW),
        P(ROW, COL),
        P(ROW, COL),
        P(COL, ROW),
        P(ROW, COL),
        P(ROW, COL),
        P(COL, ROW),
    )
    return jax.shard_map(
        on_device, mesh=sub, in_specs=placed, out_specs=P(COL, ROW), check_vma=False
    )
```

```python
import math

import jax
import jax.numpy as jnp
from jax import lax
from jax.sharding import Mesh
from jax.sharding import PartitionSpec as P

BLK = 128

ROW = ("y", "c")
COL = ("z", "x")


def widen(block_mask):
    rows_blocks, cols_blocks = block_mask.shape
    spread = jnp.broadcast_to(block_mask[:, None, :, None], (rows_blocks, BLK, cols_blocks, BLK))
    return spread.reshape(rows_blocks * BLK, cols_blocks * BLK).astype(jnp.bfloat16)


def swiglu(summed, hidden_cols):
    return (jax.nn.silu(summed[:, :hidden_cols]) * summed[:, hidden_cols:]).astype(jnp.bfloat16)


def group_size(axis):
    axes = axis if isinstance(axis, tuple) else (axis,)
    return math.prod(lax.axis_size(a) for a in axes)


def gather_a2a(x, axis):
    n = group_size(axis)
    copies = jnp.broadcast_to(x[None], (n,) + x.shape).reshape((n * x.shape[0],) + x.shape[1:])
    return lax.all_to_all(copies, axis, 0, 0, tiled=True)


def scatter_sum_a2a(x, axis, sent=jnp.float32):
    n = group_size(axis)
    got = lax.all_to_all(x.astype(sent), axis, 0, 0, tiled=True)
    return got.reshape((n, x.shape[0] // n) + x.shape[1:]).astype(jnp.float32).sum(axis=0)


def on_device(tokens, gate_weight, up_weight, down_weight, gate_mask, up_mask, down_mask):
    hidden_cols = gate_weight.shape[1]
    both_weights = jnp.concatenate(
        [gate_weight * widen(gate_mask), up_weight * widen(up_mask)], axis=1
    )
    down_eff = down_weight * widen(down_mask)
    all_tokens = gather_a2a(tokens, COL)
    n_y, n_c = lax.axis_size("y"), lax.axis_size("c")
    rows, feats = all_tokens.shape
    share = rows // (n_y * n_c)
    by_core = all_tokens.reshape(n_y, n_c, share, feats).transpose(1, 0, 2, 3).reshape(rows, feats)
    partial = jnp.dot(by_core, both_weights, preferred_element_type=jnp.float32)
    summed = scatter_sum_a2a(scatter_sum_a2a(partial, "c"), "y", sent=jnp.bfloat16)
    hidden_share = swiglu(summed, hidden_cols)
    half = gather_a2a(hidden_share, "y")
    both = gather_a2a(half, "c")
    hidden = both.reshape(n_c, n_y, share, -1).transpose(1, 0, 2, 3).reshape(rows, -1)
    partial_out = jnp.dot(hidden, down_eff, preferred_element_type=jnp.float32)
    partial_out = scatter_sum_a2a(scatter_sum_a2a(partial_out, "z", sent=jnp.bfloat16), "x")
    return partial_out.astype(jnp.bfloat16)


def solution(mesh):
    n_row, n_col = mesh.devices.shape
    n_c = 2
    n_x = 4
    sub = Mesh(
        mesh.devices.reshape(n_row // n_c, n_c, n_col // n_x, n_x), ROW + COL
    )
    placed = (
        P(COL, ROW),
        P(ROW, COL),
        P(ROW, COL),
        P(COL, ROW),
        P(ROW, COL),
        P(ROW, COL),
        P(COL, ROW),
    )
    return jax.shard_map(
        on_device, mesh=sub, in_specs=placed, out_specs=P(COL, ROW), check_vma=False
    )
```

```python
import math

import jax
import jax.numpy as jnp
from jax import lax
from jax.sharding import Mesh
from jax.sharding import PartitionSpec as P

BLK = 128

ROW = ("y", "c")
COL = ("z", "x")


def widen(block_mask):
    rows_blocks, cols_blocks = block_mask.shape
    spread = jnp.broadcast_to(block_mask[:, None, :, None], (rows_blocks, BLK, cols_blocks, BLK))
    return spread.reshape(rows_blocks * BLK, cols_blocks * BLK).astype(jnp.bfloat16)


def swiglu(summed, hidden_cols):
    return (jax.nn.silu(summed[:, :hidden_cols]) * summed[:, hidden_cols:]).astype(jnp.bfloat16)


def group_size(axis):
    axes = axis if isinstance(axis, tuple) else (axis,)
    return math.prod(lax.axis_size(a) for a in axes)


def gather_a2a(x, axis):
    n = group_size(axis)
    copies = jnp.broadcast_to(x[None], (n,) + x.shape).reshape((n * x.shape[0],) + x.shape[1:])
    return lax.all_to_all(copies, axis, 0, 0, tiled=True)


def scatter_sum_a2a(x, axis, sent=jnp.float32):
    n = group_size(axis)
    got = lax.all_to_all(x.astype(sent), axis, 0, 0, tiled=True)
    return got.reshape((n, x.shape[0] // n) + x.shape[1:]).astype(jnp.float32).sum(axis=0)


def on_device(tokens, gate_weight, up_weight, down_weight, gate_mask, up_mask, down_mask):
    hidden_cols = gate_weight.shape[1]
    both_weights = jnp.concatenate(
        [gate_weight * widen(gate_mask), up_weight * widen(up_mask)], axis=1
    )
    down_eff = down_weight * widen(down_mask)
    all_tokens = gather_a2a(tokens, COL)
    n_y, n_c = lax.axis_size("y"), lax.axis_size("c")
    rows, feats = all_tokens.shape
    share = rows // (n_y * n_c)
    by_core = all_tokens.reshape(n_y, n_c, share, feats).transpose(1, 0, 2, 3).reshape(rows, feats)
    partial = jnp.dot(by_core, both_weights, preferred_element_type=jnp.float32)
    summed = scatter_sum_a2a(scatter_sum_a2a(partial, "c"), "y")
    hidden_share = swiglu(summed, hidden_cols)
    half = gather_a2a(hidden_share, "y")
    both = gather_a2a(half, "c")
    hidden = both.reshape(n_c, n_y, share, -1).transpose(1, 0, 2, 3).reshape(rows, -1)
    partial_out = jnp.dot(hidden, down_eff, preferred_element_type=jnp.float32)
    n_z, n_x = lax.axis_size("z"), lax.axis_size("x")
    out_share = rows // (n_z * n_x)
    partial_out = partial_out.reshape(n_z, n_x, out_share, -1).transpose(1, 0, 2, 3).reshape(rows, -1)
    partial_out = scatter_sum_a2a(scatter_sum_a2a(partial_out, "x"), "z", sent=jnp.bfloat16)
    return partial_out.astype(jnp.bfloat16)


def solution(mesh):
    n_row, n_col = mesh.devices.shape
    n_c = 2
    n_x = 4
    sub = Mesh(
        mesh.devices.reshape(n_row // n_c, n_c, n_col // n_x, n_x), ROW + COL
    )
    placed = (
        P(COL, ROW),
        P(ROW, COL),
        P(ROW, COL),
        P(COL, ROW),
        P(ROW, COL),
        P(ROW, COL),
        P(COL, ROW),
    )
    return jax.shard_map(
        on_device, mesh=sub, in_specs=placed, out_specs=P(COL, ROW), check_vma=False
    )
```

```python
import math

import jax
import jax.numpy as jnp
from jax import lax
from jax.sharding import Mesh
from jax.sharding import PartitionSpec as P

BLK = 128

ROW = ("y", "c")
COL = ("z", "x")


def widen(block_mask):
    rows_blocks, cols_blocks = block_mask.shape
    spread = jnp.broadcast_to(block_mask[:, None, :, None], (rows_blocks, BLK, cols_blocks, BLK))
    return spread.reshape(rows_blocks * BLK, cols_blocks * BLK).astype(jnp.bfloat16)


def scatter_sum_split(x, axis):
    cut = x.shape[-1] // 2
    first = lax.psum_scatter(x[..., :cut], axis, scatter_dimension=0, tiled=True)
    second = scatter_sum_a2a(x[..., cut:], axis)
    return jnp.concatenate([first, second], axis=-1)


def swiglu(summed, hidden_cols):
    return (jax.nn.silu(summed[:, :hidden_cols]) * summed[:, hidden_cols:]).astype(jnp.bfloat16)


def group_size(axis):
    axes = axis if isinstance(axis, tuple) else (axis,)
    return math.prod(lax.axis_size(a) for a in axes)


def gather_a2a(x, axis):
    n = group_size(axis)
    copies = jnp.broadcast_to(x[None], (n,) + x.shape).reshape((n * x.shape[0],) + x.shape[1:])
    return lax.all_to_all(copies, axis, 0, 0, tiled=True)


def scatter_sum_a2a(x, axis, sent=jnp.float32):
    n = group_size(axis)
    got = lax.all_to_all(x.astype(sent), axis, 0, 0, tiled=True)
    return got.reshape((n, x.shape[0] // n) + x.shape[1:]).astype(jnp.float32).sum(axis=0)


def on_device(tokens, gate_weight, up_weight, down_weight, gate_mask, up_mask, down_mask):
    hidden_cols = gate_weight.shape[1]
    both_weights = jnp.concatenate(
        [gate_weight * widen(gate_mask), up_weight * widen(up_mask)], axis=1
    )
    down_eff = down_weight * widen(down_mask)
    all_tokens = gather_a2a(tokens, COL)
    n_y, n_c = lax.axis_size("y"), lax.axis_size("c")
    rows, feats = all_tokens.shape
    share = rows // (n_y * n_c)
    by_core = all_tokens.reshape(n_y, n_c, share, feats).transpose(1, 0, 2, 3).reshape(rows, feats)
    partial = jnp.dot(by_core, both_weights, preferred_element_type=jnp.float32)
    summed = scatter_sum_split(scatter_sum_a2a(partial, "c"), "y")
    hidden_share = swiglu(summed, hidden_cols)
    half = gather_a2a(hidden_share, "y")
    both = gather_a2a(half, "c")
    hidden = both.reshape(n_c, n_y, share, -1).transpose(1, 0, 2, 3).reshape(rows, -1)
    partial_out = jnp.dot(hidden, down_eff, preferred_element_type=jnp.float32)
    n_z, n_x = lax.axis_size("z"), lax.axis_size("x")
    out_share = rows // (n_z * n_x)
    partial_out = partial_out.reshape(n_z, n_x, out_share, -1).transpose(1, 0, 2, 3).reshape(rows, -1)
    partial_out = scatter_sum_a2a(scatter_sum_split(partial_out, "x"), "z", sent=jnp.bfloat16)
    return partial_out.astype(jnp.bfloat16)


def solution(mesh):
    n_row, n_col = mesh.devices.shape
    n_c = 2
    n_x = 4
    sub = Mesh(
        mesh.devices.reshape(n_row // n_c, n_c, n_col // n_x, n_x), ROW + COL
    )
    placed = (
        P(COL, ROW),
        P(ROW, COL),
        P(ROW, COL),
        P(COL, ROW),
        P(ROW, COL),
        P(ROW, COL),
        P(COL, ROW),
    )
    return jax.shard_map(
        on_device, mesh=sub, in_specs=placed, out_specs=P(COL, ROW), check_vma=False
    )
```

```python
import math

import jax
import jax.numpy as jnp
from jax import lax
from jax.sharding import Mesh
from jax.sharding import PartitionSpec as P

BLK = 128

ROW = ("y", "c")
COL = ("z", "x")


def widen(block_mask):
    rows_blocks, cols_blocks = block_mask.shape
    spread = jnp.broadcast_to(block_mask[:, None, :, None], (rows_blocks, BLK, cols_blocks, BLK))
    return spread.reshape(rows_blocks * BLK, cols_blocks * BLK).astype(jnp.bfloat16)


def scatter_sum_split(x, axis):
    cut = x.shape[-1] // 2
    first = lax.psum_scatter(x[..., :cut], axis, scatter_dimension=0, tiled=True)
    second = scatter_sum_a2a(x[..., cut:], axis)
    return jnp.concatenate([first, second], axis=-1)


def swiglu(summed, hidden_cols):
    return (jax.nn.silu(summed[:, :hidden_cols]) * summed[:, hidden_cols:]).astype(jnp.bfloat16)


def group_size(axis):
    axes = axis if isinstance(axis, tuple) else (axis,)
    return math.prod(lax.axis_size(a) for a in axes)


def gather_a2a(x, axis):
    n = group_size(axis)
    copies = jnp.broadcast_to(x[None], (n,) + x.shape).reshape((n * x.shape[0],) + x.shape[1:])
    return lax.all_to_all(copies, axis, 0, 0, tiled=True)


def scatter_sum_a2a(x, axis, sent=jnp.float32):
    n = group_size(axis)
    got = lax.all_to_all(x.astype(sent), axis, 0, 0, tiled=True)
    return got.reshape((n, x.shape[0] // n) + x.shape[1:]).astype(jnp.float32).sum(axis=0)


N_CHUNK = 2


def layer_chunk(tokens, both_weights, down_eff, hidden_cols):
    all_tokens = gather_a2a(tokens, COL)
    n_y, n_c = lax.axis_size("y"), lax.axis_size("c")
    rows, feats = all_tokens.shape
    share = rows // (n_y * n_c)
    by_core = all_tokens.reshape(n_y, n_c, share, feats).transpose(1, 0, 2, 3).reshape(rows, feats)
    partial = jnp.dot(by_core, both_weights, preferred_element_type=jnp.float32)
    summed = lax.psum_scatter(scatter_sum_a2a(partial, "c"), "y", scatter_dimension=0, tiled=True)
    hidden_share = swiglu(summed, hidden_cols)
    half = gather_a2a(hidden_share, "y")
    both = gather_a2a(half, "c")
    hidden = both.reshape(n_c, n_y, share, -1).transpose(1, 0, 2, 3).reshape(rows, -1)
    partial_out = jnp.dot(hidden, down_eff, preferred_element_type=jnp.float32)
    n_z, n_x = lax.axis_size("z"), lax.axis_size("x")
    out_share = rows // (n_z * n_x)
    partial_out = partial_out.reshape(n_z, n_x, out_share, -1).transpose(1, 0, 2, 3).reshape(rows, -1)
    return scatter_sum_a2a(scatter_sum_a2a(partial_out, "x"), "z", sent=jnp.bfloat16)


def on_device(tokens, gate_weight, up_weight, down_weight, gate_mask, up_mask, down_mask):
    hidden_cols = gate_weight.shape[1]
    both_weights = jnp.concatenate(
        [gate_weight * widen(gate_mask), up_weight * widen(up_mask)], axis=1
    )
    down_eff = down_weight * widen(down_mask)
    step = tokens.shape[0] // N_CHUNK
    outs = [
        layer_chunk(tokens[k * step:(k + 1) * step], both_weights, down_eff, hidden_cols)
        for k in range(N_CHUNK)
    ]
    return jnp.concatenate(outs, axis=0).astype(jnp.bfloat16)


def solution(mesh):
    n_row, n_col = mesh.devices.shape
    n_c = 2
    n_x = 4
    sub = Mesh(
        mesh.devices.reshape(n_row // n_c, n_c, n_col // n_x, n_x), ROW + COL
    )
    placed = (
        P(COL, ROW),
        P(ROW, COL),
        P(ROW, COL),
        P(COL, ROW),
        P(ROW, COL),
        P(ROW, COL),
        P(COL, ROW),
    )
    return jax.shard_map(
        on_device, mesh=sub, in_specs=placed, out_specs=P(COL, ROW), check_vma=False
    )
```

```python
import math

import jax
import jax.numpy as jnp
from jax import lax
from jax.sharding import Mesh
from jax.sharding import PartitionSpec as P

BLK = 128

ROW = ("y", "c")
COL = ("z", "x")


def widen(block_mask):
    rows_blocks, cols_blocks = block_mask.shape
    spread = jnp.broadcast_to(block_mask[:, None, :, None], (rows_blocks, BLK, cols_blocks, BLK))
    return spread.reshape(rows_blocks * BLK, cols_blocks * BLK).astype(jnp.bfloat16)


def swiglu(summed, hidden_cols):
    return (jax.nn.silu(summed[:, :hidden_cols]) * summed[:, hidden_cols:]).astype(jnp.bfloat16)


def group_size(axis):
    axes = axis if isinstance(axis, tuple) else (axis,)
    return math.prod(lax.axis_size(a) for a in axes)


def gather_a2a(x, axis):
    n = group_size(axis)
    copies = jnp.broadcast_to(x[None], (n,) + x.shape).reshape((n * x.shape[0],) + x.shape[1:])
    return lax.all_to_all(copies, axis, 0, 0, tiled=True)


def scatter_sum_a2a(x, axis, sent=jnp.float32):
    n = group_size(axis)
    got = lax.all_to_all(x.astype(sent), axis, 0, 0, tiled=True)
    return got.reshape((n, x.shape[0] // n) + x.shape[1:]).astype(jnp.float32).sum(axis=0)


def on_device(tokens, gate_weight, up_weight, down_weight, gate_mask, up_mask, down_mask):
    hidden_cols = gate_weight.shape[1]
    both_weights = jnp.concatenate(
        [gate_weight * widen(gate_mask), up_weight * widen(up_mask)], axis=1
    )
    down_eff = down_weight * widen(down_mask)
    all_tokens = gather_a2a(tokens, COL)
    n_y, n_c = lax.axis_size("y"), lax.axis_size("c")
    rows, feats = all_tokens.shape
    share = rows // (n_y * n_c)
    by_core = all_tokens.reshape(n_y, n_c, share, feats).transpose(1, 0, 2, 3).reshape(rows, feats)
    partial = jnp.dot(by_core, both_weights, preferred_element_type=jnp.float32)
    summed = scatter_sum_a2a(scatter_sum_a2a(partial, "c"), "y")
    hidden_share = swiglu(summed, hidden_cols)
    half = gather_a2a(hidden_share, "y")
    both = gather_a2a(half, "c")
    hidden = both.reshape(n_c, n_y, share, -1).transpose(1, 0, 2, 3).reshape(rows, -1)
    partial_out = jnp.dot(hidden, down_eff, preferred_element_type=jnp.float32)
    partial_out = scatter_sum_a2a(partial_out, COL, sent=jnp.bfloat16)
    return partial_out.astype(jnp.bfloat16)


def solution(mesh):
    n_row, n_col = mesh.devices.shape
    n_c = 2
    n_x = 4
    sub = Mesh(
        mesh.devices.reshape(n_row // n_c, n_c, n_col // n_x, n_x), ROW + COL
    )
    placed = (
        P(COL, ROW),
        P(ROW, COL),
        P(ROW, COL),
        P(COL, ROW),
        P(ROW, COL),
        P(ROW, COL),
        P(COL, ROW),
    )
    return jax.shard_map(
        on_device, mesh=sub, in_specs=placed, out_specs=P(COL, ROW), check_vma=False
    )
```

```python
import math

import jax
import jax.numpy as jnp
from jax import lax
from jax.sharding import Mesh
from jax.sharding import PartitionSpec as P

BLK = 128

ROW = ("y", "c")
COL = ("z", "x")


def widen(block_mask):
    rows_blocks, cols_blocks = block_mask.shape
    spread = jnp.broadcast_to(block_mask[:, None, :, None], (rows_blocks, BLK, cols_blocks, BLK))
    return spread.reshape(rows_blocks * BLK, cols_blocks * BLK).astype(jnp.bfloat16)


def shift(x, axis, step):
    n = lax.axis_size(axis)
    return lax.ppermute(x, axis, [(s, (s + step) % n) for s in range(n)])


def scatter_sum_chains(x, axis):
    n = lax.axis_size(axis)
    i = lax.axis_index(axis)
    blocks = x.reshape((n, x.shape[0] // n) + x.shape[1:])
    own = lambda k: lax.dynamic_index_in_dim(blocks, k % n, axis=0, keepdims=False)
    up_steps, down_steps = (n - 1) // 2, n // 2
    acc_up = own(i + up_steps)
    for s in range(1, up_steps + 1):
        got = shift(acc_up, axis, 1)
        acc_up = got + own(i + up_steps - s) if s < up_steps else got
    acc_down = own(i - down_steps)
    for s in range(1, down_steps + 1):
        got = shift(acc_down, axis, -1)
        acc_down = got + own(i - down_steps + s) if s < down_steps else got
    return acc_up + acc_down + own(i)


def swiglu(summed, hidden_cols):
    return (jax.nn.silu(summed[:, :hidden_cols]) * summed[:, hidden_cols:]).astype(jnp.bfloat16)


def group_size(axis):
    axes = axis if isinstance(axis, tuple) else (axis,)
    return math.prod(lax.axis_size(a) for a in axes)


def gather_a2a(x, axis):
    n = group_size(axis)
    copies = jnp.broadcast_to(x[None], (n,) + x.shape).reshape((n * x.shape[0],) + x.shape[1:])
    return lax.all_to_all(copies, axis, 0, 0, tiled=True)


def scatter_sum_a2a(x, axis, sent=jnp.float32):
    n = group_size(axis)
    got = lax.all_to_all(x.astype(sent), axis, 0, 0, tiled=True)
    return got.reshape((n, x.shape[0] // n) + x.shape[1:]).astype(jnp.float32).sum(axis=0)


def on_device(tokens, gate_weight, up_weight, down_weight, gate_mask, up_mask, down_mask):
    hidden_cols = gate_weight.shape[1]
    both_weights = jnp.concatenate(
        [gate_weight * widen(gate_mask), up_weight * widen(up_mask)], axis=1
    )
    down_eff = down_weight * widen(down_mask)
    all_tokens = gather_a2a(tokens, COL)
    n_y, n_c = lax.axis_size("y"), lax.axis_size("c")
    rows, feats = all_tokens.shape
    share = rows // (n_y * n_c)
    by_core = all_tokens.reshape(n_y, n_c, share, feats).transpose(1, 0, 2, 3).reshape(rows, feats)
    partial = jnp.dot(by_core, both_weights, preferred_element_type=jnp.float32)
    summed = scatter_sum_chains(scatter_sum_a2a(partial, "c"), "y")
    hidden_share = swiglu(summed, hidden_cols)
    half = gather_a2a(hidden_share, "y")
    both = gather_a2a(half, "c")
    hidden = both.reshape(n_c, n_y, share, -1).transpose(1, 0, 2, 3).reshape(rows, -1)
    partial_out = jnp.dot(hidden, down_eff, preferred_element_type=jnp.float32)
    partial_out = scatter_sum_a2a(partial_out, COL, sent=jnp.bfloat16)
    return partial_out.astype(jnp.bfloat16)


def solution(mesh):
    n_row, n_col = mesh.devices.shape
    n_c = 2
    n_x = 4
    sub = Mesh(
        mesh.devices.reshape(n_row // n_c, n_c, n_col // n_x, n_x), ROW + COL
    )
    placed = (
        P(COL, ROW),
        P(ROW, COL),
        P(ROW, COL),
        P(COL, ROW),
        P(ROW, COL),
        P(ROW, COL),
        P(COL, ROW),
    )
    return jax.shard_map(
        on_device, mesh=sub, in_specs=placed, out_specs=P(COL, ROW), check_vma=False
    )
```

```python
import math

import jax
import jax.numpy as jnp
from jax import lax
from jax.sharding import Mesh
from jax.sharding import PartitionSpec as P

BLK = 128

ROW = ("y", "c")
COL = ("z", "x")


def widen(block_mask):
    rows_blocks, cols_blocks = block_mask.shape
    spread = jnp.broadcast_to(block_mask[:, None, :, None], (rows_blocks, BLK, cols_blocks, BLK))
    return spread.reshape(rows_blocks * BLK, cols_blocks * BLK).astype(jnp.bfloat16)


def shift(x, axis, step):
    n = lax.axis_size(axis)
    return lax.ppermute(x, axis, [(s, (s + step) % n) for s in range(n)])


def scatter_sum_chains(x, axis):
    n = lax.axis_size(axis)
    i = lax.axis_index(axis)
    blocks = x.reshape((n, x.shape[0] // n) + x.shape[1:])
    own = lambda k: lax.dynamic_index_in_dim(blocks, k % n, axis=0, keepdims=False)
    up_steps, down_steps = (n - 1) // 2, n // 2
    acc_up = own(i + up_steps)
    for s in range(1, up_steps + 1):
        got = shift(acc_up, axis, 1)
        acc_up = got + own(i + up_steps - s) if s < up_steps else got
    acc_down = own(i - down_steps)
    for s in range(1, down_steps + 1):
        got = shift(acc_down, axis, -1)
        acc_down = got + own(i - down_steps + s) if s < down_steps else got
    return acc_up + acc_down + own(i)


def scatter_sum_pair(x, axis):
    i = lax.axis_index(axis)
    halves = x.reshape((2, x.shape[0] // 2) + x.shape[1:])
    mine = lax.dynamic_index_in_dim(halves, i, axis=0, keepdims=False)
    theirs = lax.dynamic_index_in_dim(halves, 1 - i, axis=0, keepdims=False)
    return mine + shift(theirs, axis, 1)


def gather_pair(x, axis):
    i = lax.axis_index(axis)
    parts = jnp.stack([x, shift(x, axis, 1)])
    return jnp.take(parts, (i - jnp.arange(2)) % 2, axis=0).reshape((2 * x.shape[0],) + x.shape[1:])


def swiglu(summed, hidden_cols):
    return (jax.nn.silu(summed[:, :hidden_cols]) * summed[:, hidden_cols:]).astype(jnp.bfloat16)


def group_size(axis):
    axes = axis if isinstance(axis, tuple) else (axis,)
    return math.prod(lax.axis_size(a) for a in axes)


def gather_a2a(x, axis):
    n = group_size(axis)
    copies = jnp.broadcast_to(x[None], (n,) + x.shape).reshape((n * x.shape[0],) + x.shape[1:])
    return lax.all_to_all(copies, axis, 0, 0, tiled=True)


def scatter_sum_a2a(x, axis, sent=jnp.float32):
    n = group_size(axis)
    got = lax.all_to_all(x.astype(sent), axis, 0, 0, tiled=True)
    return got.reshape((n, x.shape[0] // n) + x.shape[1:]).astype(jnp.float32).sum(axis=0)


def on_device(tokens, gate_weight, up_weight, down_weight, gate_mask, up_mask, down_mask):
    hidden_cols = gate_weight.shape[1]
    both_weights = jnp.concatenate(
        [gate_weight * widen(gate_mask), up_weight * widen(up_mask)], axis=1
    )
    down_eff = down_weight * widen(down_mask)
    all_tokens = gather_a2a(tokens, COL)
    n_y, n_c = lax.axis_size("y"), lax.axis_size("c")
    rows, feats = all_tokens.shape
    share = rows // (n_y * n_c)
    by_core = all_tokens.reshape(n_y, n_c, share, feats).transpose(1, 0, 2, 3).reshape(rows, feats)
    partial = jnp.dot(by_core, both_weights, preferred_element_type=jnp.float32)
    summed = scatter_sum_chains(scatter_sum_pair(partial, "c"), "y")
    hidden_share = swiglu(summed, hidden_cols)
    half = gather_a2a(hidden_share, "y")
    both = gather_pair(half, "c")
    hidden = both.reshape(n_c, n_y, share, -1).transpose(1, 0, 2, 3).reshape(rows, -1)
    partial_out = jnp.dot(hidden, down_eff, preferred_element_type=jnp.float32)
    partial_out = scatter_sum_a2a(partial_out, COL, sent=jnp.bfloat16)
    return partial_out.astype(jnp.bfloat16)


def solution(mesh):
    n_row, n_col = mesh.devices.shape
    n_c = 2
    n_x = 4
    sub = Mesh(
        mesh.devices.reshape(n_row // n_c, n_c, n_col // n_x, n_x), ROW + COL
    )
    placed = (
        P(COL, ROW),
        P(ROW, COL),
        P(ROW, COL),
        P(COL, ROW),
        P(ROW, COL),
        P(ROW, COL),
        P(COL, ROW),
    )
    return jax.shard_map(
        on_device, mesh=sub, in_specs=placed, out_specs=P(COL, ROW), check_vma=False
    )
```

```python
import math

import jax
import jax.numpy as jnp
from jax import lax
from jax.sharding import Mesh
from jax.sharding import PartitionSpec as P

BLK = 128

ROW = ("y", "c")
COL = ("z", "x")


def widen(block_mask):
    rows_blocks, cols_blocks = block_mask.shape
    spread = jnp.broadcast_to(block_mask[:, None, :, None], (rows_blocks, BLK, cols_blocks, BLK))
    return spread.reshape(rows_blocks * BLK, cols_blocks * BLK).astype(jnp.bfloat16)


def shift(x, axis, step):
    n = lax.axis_size(axis)
    return lax.ppermute(x, axis, [(s, (s + step) % n) for s in range(n)])


def scatter_sum_chains(x, axis):
    n = lax.axis_size(axis)
    i = lax.axis_index(axis)
    blocks = x.reshape((n, x.shape[0] // n) + x.shape[1:])
    own = lambda k: lax.dynamic_index_in_dim(blocks, k % n, axis=0, keepdims=False)
    up_steps, down_steps = (n - 1) // 2, n // 2
    acc_up = own(i + up_steps)
    for s in range(1, up_steps + 1):
        got = shift(acc_up, axis, 1)
        acc_up = got + own(i + up_steps - s) if s < up_steps else got
    acc_down = own(i - down_steps)
    for s in range(1, down_steps + 1):
        got = shift(acc_down, axis, -1)
        acc_down = got + own(i - down_steps + s) if s < down_steps else got
    return acc_up + acc_down + own(i)


def scatter_sum_pair(x, axis):
    i = lax.axis_index(axis)
    halves = x.reshape((2, x.shape[0] // 2) + x.shape[1:])
    mine = lax.dynamic_index_in_dim(halves, i, axis=0, keepdims=False)
    theirs = lax.dynamic_index_in_dim(halves, 1 - i, axis=0, keepdims=False)
    return mine + shift(theirs, axis, 1)


def gather_pair(x, axis):
    i = lax.axis_index(axis)
    parts = jnp.stack([x, shift(x, axis, 1)])
    return jnp.take(parts, (i - jnp.arange(2)) % 2, axis=0).reshape((2 * x.shape[0],) + x.shape[1:])


def swiglu(summed, hidden_cols):
    return (jax.nn.silu(summed[:, :hidden_cols]) * summed[:, hidden_cols:]).astype(jnp.bfloat16)


def group_size(axis):
    axes = axis if isinstance(axis, tuple) else (axis,)
    return math.prod(lax.axis_size(a) for a in axes)


def gather_a2a(x, axis):
    n = group_size(axis)
    copies = jnp.broadcast_to(x[None], (n,) + x.shape).reshape((n * x.shape[0],) + x.shape[1:])
    return lax.all_to_all(copies, axis, 0, 0, tiled=True)


def scatter_sum_a2a(x, axis, sent=jnp.float32):
    n = group_size(axis)
    got = lax.all_to_all(x.astype(sent), axis, 0, 0, tiled=True)
    return got.reshape((n, x.shape[0] // n) + x.shape[1:]).astype(jnp.float32).sum(axis=0)


def on_device(tokens, gate_weight, up_weight, down_weight, gate_mask, up_mask, down_mask):
    hidden_cols = gate_weight.shape[1]
    both_weights = jnp.concatenate(
        [gate_weight * widen(gate_mask), up_weight * widen(up_mask)], axis=1
    )
    down_eff = down_weight * widen(down_mask)
    all_tokens = gather_a2a(gather_a2a(tokens, "z"), "x")
    n_y, n_c = lax.axis_size("y"), lax.axis_size("c")
    rows, feats = all_tokens.shape
    share = rows // (n_y * n_c)
    by_core = all_tokens.reshape(n_y, n_c, share, feats).transpose(1, 0, 2, 3).reshape(rows, feats)
    partial = jnp.dot(by_core, both_weights, preferred_element_type=jnp.float32)
    summed = scatter_sum_chains(scatter_sum_pair(partial, "c"), "y")
    hidden_share = swiglu(summed, hidden_cols)
    half = gather_a2a(hidden_share, "y")
    both = gather_pair(half, "c")
    hidden = both.reshape(n_c, n_y, share, -1).transpose(1, 0, 2, 3).reshape(rows, -1)
    partial_out = jnp.dot(hidden, down_eff, preferred_element_type=jnp.float32)
    partial_out = scatter_sum_a2a(scatter_sum_a2a(partial_out, "x", sent=jnp.bfloat16), "z")
    return partial_out.astype(jnp.bfloat16)


def solution(mesh):
    n_row, n_col = mesh.devices.shape
    n_c = 2
    n_x = 4
    sub = Mesh(
        mesh.devices.reshape(n_row // n_c, n_c, n_col // n_x, n_x), ROW + COL
    )
    placed = (
        P(COL, ROW),
        P(ROW, COL),
        P(ROW, COL),
        P(COL, ROW),
        P(ROW, COL),
        P(ROW, COL),
        P(COL, ROW),
    )
    return jax.shard_map(
        on_device, mesh=sub, in_specs=placed, out_specs=P(COL, ROW), check_vma=False
    )
```

```python
import math

import jax
import jax.numpy as jnp
from jax import lax
from jax.sharding import Mesh
from jax.sharding import PartitionSpec as P

BLK = 128

ROW = ("y", "c")
COL = ("z", "x")


def widen(block_mask):
    rows_blocks, cols_blocks = block_mask.shape
    spread = jnp.broadcast_to(block_mask[:, None, :, None], (rows_blocks, BLK, cols_blocks, BLK))
    return spread.reshape(rows_blocks * BLK, cols_blocks * BLK).astype(jnp.bfloat16)


def shift(x, axis, step):
    n = lax.axis_size(axis)
    return lax.ppermute(x, axis, [(s, (s + step) % n) for s in range(n)])


def scatter_sum_chains(x, axis):
    n = lax.axis_size(axis)
    i = lax.axis_index(axis)
    blocks = x.reshape((n, x.shape[0] // n) + x.shape[1:])
    own = lambda k: lax.dynamic_index_in_dim(blocks, k % n, axis=0, keepdims=False)
    up_steps, down_steps = (n - 1) // 2, n // 2
    acc_up = own(i + up_steps)
    for s in range(1, up_steps + 1):
        got = shift(acc_up, axis, 1)
        acc_up = got + own(i + up_steps - s) if s < up_steps else got
    acc_down = own(i - down_steps)
    for s in range(1, down_steps + 1):
        got = shift(acc_down, axis, -1)
        acc_down = got + own(i - down_steps + s) if s < down_steps else got
    return acc_up + acc_down + own(i)


def scatter_sum_pair(x, axis):
    i = lax.axis_index(axis)
    halves = x.reshape((2, x.shape[0] // 2) + x.shape[1:])
    mine = lax.dynamic_index_in_dim(halves, i, axis=0, keepdims=False)
    theirs = lax.dynamic_index_in_dim(halves, 1 - i, axis=0, keepdims=False)
    return mine + shift(theirs, axis, 1)


def gather_pair(x, axis):
    i = lax.axis_index(axis)
    parts = jnp.stack([x, shift(x, axis, 1)])
    return jnp.take(parts, (i - jnp.arange(2)) % 2, axis=0).reshape((2 * x.shape[0],) + x.shape[1:])


def swiglu(summed, hidden_cols):
    return (jax.nn.silu(summed[:, :hidden_cols]) * summed[:, hidden_cols:]).astype(jnp.bfloat16)


def group_size(axis):
    axes = axis if isinstance(axis, tuple) else (axis,)
    return math.prod(lax.axis_size(a) for a in axes)


def gather_a2a(x, axis):
    n = group_size(axis)
    copies = jnp.broadcast_to(x[None], (n,) + x.shape).reshape((n * x.shape[0],) + x.shape[1:])
    return lax.all_to_all(copies, axis, 0, 0, tiled=True)


def scatter_sum_a2a(x, axis, sent=jnp.float32):
    n = group_size(axis)
    got = lax.all_to_all(x.astype(sent), axis, 0, 0, tiled=True)
    return got.reshape((n, x.shape[0] // n) + x.shape[1:]).astype(jnp.float32).sum(axis=0)


def on_device(tokens, gate_weight, up_weight, down_weight, gate_mask, up_mask, down_mask):
    hidden_cols = gate_weight.shape[1]
    both_weights = jnp.concatenate(
        [gate_weight * widen(gate_mask), up_weight * widen(up_mask)], axis=1
    )
    down_eff = down_weight * widen(down_mask)
    all_tokens = gather_a2a(gather_a2a(tokens, "z"), "x")
    n_y, n_c = lax.axis_size("y"), lax.axis_size("c")
    rows, feats = all_tokens.shape
    share = rows // (n_y * n_c)
    by_core = all_tokens.reshape(n_y, n_c, share, feats).transpose(1, 0, 2, 3).reshape(rows, feats)
    partial = jnp.dot(by_core, both_weights, preferred_element_type=jnp.float32)
    summed = scatter_sum_chains(scatter_sum_pair(partial, "c"), "y")
    hidden_share = swiglu(summed, hidden_cols)
    half = gather_a2a(hidden_share, "y")
    both = gather_pair(half, "c")
    hidden = both.reshape(n_c, n_y, share, -1).transpose(1, 0, 2, 3).reshape(rows, -1)
    partial_out = jnp.dot(hidden, down_eff, preferred_element_type=jnp.float32)
    partial_out = scatter_sum_a2a(partial_out, ("x", "z"), sent=jnp.bfloat16)
    return partial_out.astype(jnp.bfloat16)


def solution(mesh):
    n_row, n_col = mesh.devices.shape
    n_c = 2
    n_x = 4
    sub = Mesh(
        mesh.devices.reshape(n_row // n_c, n_c, n_col // n_x, n_x), ROW + COL
    )
    placed = (
        P(COL, ROW),
        P(ROW, COL),
        P(ROW, COL),
        P(COL, ROW),
        P(ROW, COL),
        P(ROW, COL),
        P(COL, ROW),
    )
    return jax.shard_map(
        on_device, mesh=sub, in_specs=placed, out_specs=P(COL, ROW), check_vma=False
    )
```

```python
import math

import jax
import jax.numpy as jnp
from jax import lax
from jax.sharding import Mesh
from jax.sharding import PartitionSpec as P

BLK = 128

ROW = ("y", "c")
COL = ("z", "x")


def widen(block_mask):
    rows_blocks, cols_blocks = block_mask.shape
    spread = jnp.broadcast_to(block_mask[:, None, :, None], (rows_blocks, BLK, cols_blocks, BLK))
    return spread.reshape(rows_blocks * BLK, cols_blocks * BLK).astype(jnp.bfloat16)


def shift(x, axis, step):
    n = lax.axis_size(axis)
    return lax.ppermute(x, axis, [(s, (s + step) % n) for s in range(n)])


def scatter_sum_chains(x, axis):
    n = lax.axis_size(axis)
    i = lax.axis_index(axis)
    blocks = x.reshape((n, x.shape[0] // n) + x.shape[1:])
    own = lambda k: lax.dynamic_index_in_dim(blocks, k % n, axis=0, keepdims=False)
    steps = (n - 1) // 2
    acc_up = own(i + steps)
    for s in range(1, steps + 1):
        got = shift(acc_up, axis, 1)
        acc_up = got + own(i + steps - s) if s < steps else got
    acc_down = own(i - steps)
    for s in range(1, steps + 1):
        got = shift(acc_down, axis, -1)
        acc_down = got + own(i - steps + s) if s < steps else got
    total = acc_up + acc_down + own(i)
    if n % 2 == 0:
        far = own(i + n // 2)
        cut = far.shape[-1] // 2
        near = jnp.concatenate(
            [shift(far[..., :cut], axis, n // 2), shift(far[..., cut:], axis, -(n // 2))], axis=-1
        )
        total = total + near
    return total


def scatter_sum_pair(x, axis):
    i = lax.axis_index(axis)
    halves = x.reshape((2, x.shape[0] // 2) + x.shape[1:])
    mine = lax.dynamic_index_in_dim(halves, i, axis=0, keepdims=False)
    theirs = lax.dynamic_index_in_dim(halves, 1 - i, axis=0, keepdims=False)
    return mine + shift(theirs, axis, 1)


def gather_pair(x, axis):
    i = lax.axis_index(axis)
    parts = jnp.stack([x, shift(x, axis, 1)])
    return jnp.take(parts, (i - jnp.arange(2)) % 2, axis=0).reshape((2 * x.shape[0],) + x.shape[1:])


def swiglu(summed, hidden_cols):
    return (jax.nn.silu(summed[:, :hidden_cols]) * summed[:, hidden_cols:]).astype(jnp.bfloat16)


def group_size(axis):
    axes = axis if isinstance(axis, tuple) else (axis,)
    return math.prod(lax.axis_size(a) for a in axes)


def gather_a2a(x, axis):
    n = group_size(axis)
    copies = jnp.broadcast_to(x[None], (n,) + x.shape).reshape((n * x.shape[0],) + x.shape[1:])
    return lax.all_to_all(copies, axis, 0, 0, tiled=True)


def scatter_sum_a2a(x, axis, sent=jnp.float32):
    n = group_size(axis)
    got = lax.all_to_all(x.astype(sent), axis, 0, 0, tiled=True)
    return got.reshape((n, x.shape[0] // n) + x.shape[1:]).astype(jnp.float32).sum(axis=0)


def on_device(tokens, gate_weight, up_weight, down_weight, gate_mask, up_mask, down_mask):
    hidden_cols = gate_weight.shape[1]
    both_weights = jnp.concatenate(
        [gate_weight * widen(gate_mask), up_weight * widen(up_mask)], axis=1
    )
    down_eff = down_weight * widen(down_mask)
    all_tokens = gather_a2a(gather_a2a(tokens, "z"), "x")
    n_y, n_c = lax.axis_size("y"), lax.axis_size("c")
    rows, feats = all_tokens.shape
    share = rows // (n_y * n_c)
    by_core = all_tokens.reshape(n_y, n_c, share, feats).transpose(1, 0, 2, 3).reshape(rows, feats)
    partial = jnp.dot(by_core, both_weights, preferred_element_type=jnp.float32)
    summed = scatter_sum_chains(scatter_sum_pair(partial, "c"), "y")
    hidden_share = swiglu(summed, hidden_cols)
    half = gather_a2a(hidden_share, "y")
    both = gather_pair(half, "c")
    hidden = both.reshape(n_c, n_y, share, -1).transpose(1, 0, 2, 3).reshape(rows, -1)
    partial_out = jnp.dot(hidden, down_eff, preferred_element_type=jnp.float32)
    partial_out = scatter_sum_a2a(partial_out, ("x", "z"), sent=jnp.bfloat16)
    return partial_out.astype(jnp.bfloat16)


def solution(mesh):
    n_row, n_col = mesh.devices.shape
    n_c = 2
    n_x = 4
    sub = Mesh(
        mesh.devices.reshape(n_row // n_c, n_c, n_col // n_x, n_x), ROW + COL
    )
    placed = (
        P(COL, ROW),
        P(ROW, COL),
        P(ROW, COL),
        P(COL, ROW),
        P(ROW, COL),
        P(ROW, COL),
        P(COL, ROW),
    )
    return jax.shard_map(
        on_device, mesh=sub, in_specs=placed, out_specs=P(COL, ROW), check_vma=False
    )
```
